512 devices in a mesh: ctx: 32 (over z, core), head: 16 (over x, y).
Axes of the slice: x: 4, y: 4, z: 16, core: 2. Of those that a mesh axis runs over, the one named last changes fastest.
Arguments:
- attn_q: bfloat16 [4096, 4096], P('ctx', 'head'), may hold values from -6 to 6
- attn_k: bfloat16 [4096, 512], P('ctx'), may hold values from -6 to 6
- attn_v: bfloat16 [4096, 512], P('ctx'), may hold values from -0.375 to 0.375
- attn_cot: bfloat16 [4096, 4096], P('ctx', 'head'), may hold values from -6 to 6
- attn_lse: float32 [16, 4096], P('head'), may hold values from 3 to 6
- attn_delta: float32 [16, 4096], P('head'), may hold values from -6 to 6
- block_lists: int32 [16, 64, 4], P('head'), may hold values from 0 to 63, as said below
- gdn_q: bfloat16 [4096, 2048], P('ctx', 'head'), may hold values from -6 to 6
- gdn_k: bfloat16 [4096, 2048], P('ctx', 'head'), may hold values from -6 to 6
- gdn_v: bfloat16 [4096, 4096], P('ctx', 'head'), may hold values from -6 to 6
- decay_logit: float32 [32, 4096], P('head', 'ctx'), may hold values from -8 to 8
- write_logit: float32 [32, 4096], P('head', 'ctx'), may hold values from -6 to 6
- decay_rate: float32 [32], P('head'), may hold values from 0.00024414062 to 0.1
- write_scale: float32 [32], P('head'), may hold values from 0.05 to 1
- gdn_cot: bfloat16 [4096, 4096], P('ctx', 'head'), may hold values from -6 to 6
Outputs:
- attn_dq: float32 [4096, 4096], P('ctx', 'head')
- attn_dk: float32 [4096, 512], P('ctx')
- attn_dv: float32 [4096, 512], P('ctx')
- gdn_dq: float32 [4096, 2048], P('ctx', 'head')
- gdn_dk: float32 [4096, 2048], P('ctx', 'head')
- gdn_dv: float32 [4096, 4096], P('ctx', 'head')
- gdn_ddecay: float32 [32, 4096], P('head', 'ctx')
- gdn_dwrite: float32 [32, 4096], P('head', 'ctx')
The draws below stay inside these ranges and needn't reach their ends.
Inputs may be any that keep to these rules, and one draw needn't show every extreme that they name: `block_lists`: entries for query block b lie in 0 to b and may repeat.
All inputs are finite; a program needn't handle non-finite values.
Results may differ from the reference program's by a relative error of at most 0.00035.
Values may be sent and summed in bfloat16 or wider, within the bound.
No kernel may reach another device: no remote copies, remote signals or barrier semaphores. Data moves between devices by JAX's collectives and lax.ppermute only.
A program may use at most 128 MiB of HBM per device.

```python
import math
import jax
import jax.numpy as jnp
from jax import lax

Q_HEADS = 16
KV_HEADS = 2
HD = 256
GK_HEADS = 16
GV_HEADS = 32
GDIM = 128
BLK = 64
TOPK = 4
SPAN = 64
TOKENS = 4096


def draw_block_lists(key, part):
    n_blocks = TOKENS // BLK
    upper_bound = jnp.arange(1, n_blocks + 1, dtype=jnp.int32)[None, :, None]
    return jax.random.randint(key, (Q_HEADS, n_blocks, TOPK), 0, upper_bound, dtype=jnp.int32)


def block_levels(rng, dims, pieces, low, top_value):
    loudness = 1.0
    for dim, shards_of in pieces:
        draws = jax.random.uniform(jax.random.fold_in(jax.random.fold_in(rng, 6), dim), (shards_of,), jnp.float32, low / len(pieces), top_value / len(pieces))
        loudness = loudness * jnp.repeat(jnp.exp(draws), dims[dim] // shards_of).reshape((-1,) + (1,) * (len(dims) - 1 - dim))
    return loudness


def gaussian(key, dims, width, reach, pieces=(), kind=jnp.bfloat16):
    result = width * jax.random.normal(key, dims, jnp.float32)
    if pieces:
        result = result * block_levels(key, dims, pieces, -0.22, 0.18)
    return jnp.clip(result, -reach, reach).astype(kind)


def setup_inputs(seed: int = 0) -> dict:
    seeds = jax.random.split(jax.random.key(seed), 16)
    attn_q = gaussian(seeds[0], (TOKENS, Q_HEADS * HD), 1.0, 6.0, ((0, 32), (1, 16)))
    attn_k = gaussian(seeds[1], (TOKENS, KV_HEADS * HD), 1.0, 6.0, ((0, 32),))
    attn_v = gaussian(seeds[2], (TOKENS, KV_HEADS * HD), 0.0625, 0.375, ((0, 32),))
    attn_cot = gaussian(seeds[3], (TOKENS, Q_HEADS * HD), 1.0, 6.0, ((0, 32), (1, 16)))
    attn_lse = jnp.clip(3.0 + 3.0 * jax.random.uniform(seeds[4], (Q_HEADS, TOKENS), jnp.float32) ** block_levels(seeds[4], (Q_HEADS, TOKENS), ((0, 16),), -0.2, 0.2), 3.0, 6.0)
    attn_delta = gaussian(seeds[5], (Q_HEADS, TOKENS), 1.0, 6.0, ((0, 16),), jnp.float32)
    block_lists = draw_block_lists(jax.random.fold_in(seeds[15], 71), 0)
    gdn_q = gaussian(seeds[7], (TOKENS, GK_HEADS * GDIM), 1.0, 6.0, ((0, 32), (1, 16)))
    gdn_k = gaussian(seeds[8], (TOKENS, GK_HEADS * GDIM), 1.0, 6.0, ((0, 32), (1, 16)))
    gdn_v = gaussian(seeds[9], (TOKENS, GV_HEADS * GDIM), 1.0, 6.0, ((0, 32), (1, 16)))
    decay_logit = gaussian(seeds[10], (GV_HEADS, TOKENS), 1.5, 8.0, ((0, 16), (1, 32)), jnp.float32)
    write_logit = gaussian(seeds[11], (GV_HEADS, TOKENS), 1.0, 6.0, ((0, 16), (1, 32)), jnp.float32)
    decay_rate = jnp.clip(jnp.exp(math.log(0.1) - 6.015181 * jax.random.uniform(seeds[12], (GV_HEADS,), jnp.float32) ** block_levels(seeds[12], (GV_HEADS,), ((0, 16),), -0.2, 0.2)), 0.00024414062, 0.1)
    write_scale = jnp.clip(jnp.exp(math.log(1.0) - 2.9957323 * jax.random.uniform(seeds[13], (GV_HEADS,), jnp.float32) ** block_levels(seeds[13], (GV_HEADS,), ((0, 16),), -0.2, 0.2)), 0.05, 1.0)
    gdn_cot = gaussian(seeds[14], (TOKENS, GV_HEADS * GDIM), 1.0, 6.0, ((0, 32), (1, 16)))
    return {"attn_q": attn_q, "attn_k": attn_k, "attn_v": attn_v, "attn_cot": attn_cot, "attn_lse": attn_lse, "attn_delta": attn_delta, "block_lists": block_lists, "gdn_q": gdn_q, "gdn_k": gdn_k, "gdn_v": gdn_v, "decay_logit": decay_logit, "write_logit": write_logit, "decay_rate": decay_rate, "write_scale": write_scale, "gdn_cot": gdn_cot}


HIGHEST = lax.Precision.HIGHEST

def unit_rows(matrix):
    return matrix / jnp.sqrt(lax.optimization_barrier(jnp.sum(matrix * matrix, axis=-1, keepdims=True)) + 1e-06)

def span_update(memory, packed):
    queries, keys_in, values_in, log_decay, write_gain = packed
    length = log_decay.shape[-1]
    cum_log = jnp.cumsum(log_decay, axis=-1)
    log_gap = cum_log[:, :, None] - cum_log[:, None, :]
    order_ids = jnp.arange(length)
    strict_low = order_ids[:, None] > order_ids[None, :]
    with_diag = order_ids[:, None] >= order_ids[None, :]
    decay_strict = jnp.where(strict_low, jnp.exp(jnp.where(strict_low, log_gap, 0.0)), 0.0)
    decay_upto = jnp.where(with_diag, jnp.exp(jnp.where(with_diag, log_gap, 0.0)), 0.0)
    key_gram = jnp.einsum('htd,hsd->hts', keys_in, keys_in, precision=HIGHEST)
    system = write_gain[:, :, None] * decay_strict * key_gram + jnp.eye(length, dtype=jnp.float32)
    decay_now = jnp.exp(cum_log)
    recalled = jnp.einsum('hvd,htd->htv', memory, keys_in, precision=HIGHEST)
    target = write_gain[:, :, None] * (values_in - decay_now[:, :, None] * recalled)
    written = lax.linalg.triangular_solve(system, target, left_side=True, lower=True, unit_diagonal=True)
    read_old = jnp.einsum('hvd,htd->htv', memory, queries, precision=HIGHEST)
    query_key = jnp.einsum('htd,hsd->hts', queries, keys_in, precision=HIGHEST)
    outputs = decay_now[:, :, None] * read_old + jnp.einsum('hts,hsv->htv', decay_upto * query_key, written, precision=HIGHEST)
    tail_decay = jnp.exp(cum_log[:, -1:] - cum_log)
    memory_next = jnp.exp(cum_log[:, -1])[:, None, None] * memory + jnp.einsum('hsv,hsd->hvd', written * tail_decay[:, :, None], keys_in, precision=HIGHEST)
    return (memory_next, outputs)

def delta_forward(raw_inputs, memory, rate_heads, scale_heads):
    query_raw, key_raw, value_raw, decay_in, write_in = raw_inputs
    n_tokens = query_raw.shape[0]
    key_heads = query_raw.shape[1] // GDIM
    value_heads = value_raw.shape[1] // GDIM
    ratio_heads = value_heads // key_heads
    n_spans = n_tokens // SPAN
    queries = jnp.repeat(unit_rows(query_raw.reshape(n_tokens, key_heads, GDIM)), ratio_heads, axis=1)
    keys_norm = jnp.repeat(unit_rows(key_raw.reshape(n_tokens, key_heads, GDIM)), ratio_heads, axis=1)
    values_in = value_raw.reshape(n_tokens, value_heads, GDIM)
    log_decay = -rate_heads[:, None] * jax.nn.softplus(decay_in)
    write_gain = scale_heads[:, None] * jax.nn.sigmoid(write_in)

    def blocks_of(tensor):
        return tensor.reshape(n_spans, SPAN, value_heads, GDIM).transpose(0, 2, 1, 3)

    def gates_of(tensor):
        return tensor.reshape(value_heads, n_spans, SPAN).transpose(1, 0, 2)
    memory_end, outputs = lax.scan(span_update, memory, (blocks_of(queries), blocks_of(keys_norm), blocks_of(values_in), gates_of(log_decay), gates_of(write_gain)))
    return (outputs.transpose(0, 2, 1, 3).reshape(n_tokens, value_heads * GDIM), memory_end)

def sparse_terms(q_blocks, cot_blocks, own_keys, own_values, listed_keys, listed_values, lse_rows, delta_rows, head_lists, block_ids):
    score_scale = HD ** (-0.5)
    q_full = q_blocks.astype(jnp.float32)
    cot_full = cot_blocks.astype(jnp.float32)
    own_kf = own_keys.astype(jnp.float32)
    own_vf = own_values.astype(jnp.float32)
    list_kf = listed_keys.astype(jnp.float32)
    list_vf = listed_values.astype(jnp.float32)
    position = jnp.arange(BLK)
    causal = position[:, None] >= position[None, :]
    slot_ids = jnp.arange(TOPK)
    repeated = jnp.any((head_lists[:, :, None] == head_lists[:, None, :]) & (slot_ids[:, None] > slot_ids[None, :]), axis=2)
    usable = (head_lists < block_ids[:, None]) & jnp.logical_not(repeated)
    own_score = jnp.einsum('bid,bjd->bij', q_full, own_kf, precision=HIGHEST) * score_scale
    list_score = jnp.einsum('bid,btjd->bitj', q_full, list_kf, precision=HIGHEST) * score_scale
    own_prob = jnp.where(causal[None], jnp.exp(own_score - lse_rows[:, :, None]), 0.0)
    list_prob = jnp.where(usable[:, None, :, None], jnp.exp(list_score - lse_rows[:, :, None, None]), 0.0)
    own_dprob = jnp.einsum('bid,bjd->bij', cot_full, own_vf, precision=HIGHEST)
    list_dprob = jnp.einsum('bid,btjd->bitj', cot_full, list_vf, precision=HIGHEST)
    own_dscore = own_prob * (own_dprob - delta_rows[:, :, None])
    list_dscore = list_prob * (list_dprob - delta_rows[:, :, None, None])
    grad_query = (jnp.einsum('bij,bjd->bid', own_dscore, own_kf, precision=HIGHEST) + jnp.einsum('bitj,btjd->bid', list_dscore, list_kf, precision=HIGHEST)) * score_scale
    own_gk = jnp.einsum('bij,bid->bjd', own_dscore, q_full, precision=HIGHEST) * score_scale
    list_gk = jnp.einsum('bitj,bid->btjd', list_dscore, q_full, precision=HIGHEST) * score_scale
    own_gv = jnp.einsum('bij,bid->bjd', own_prob, cot_full, precision=HIGHEST)
    list_gv = jnp.einsum('bitj,bid->btjd', list_prob, cot_full, precision=HIGHEST)
    return (grad_query, own_gk, list_gk, own_gv, list_gv)

def attention_grads(attn_q, attn_k, attn_v, attn_cot, attn_lse, attn_delta, block_lists):
    n_blocks = TOKENS // BLK
    group_size = Q_HEADS // KV_HEADS
    block_ids = jnp.arange(n_blocks, dtype=jnp.int32)
    key_blocks = attn_k.reshape(n_blocks, BLK, KV_HEADS, HD).transpose(2, 0, 1, 3)
    value_blocks = attn_v.reshape(n_blocks, BLK, KV_HEADS, HD).transpose(2, 0, 1, 3)

    def per_head(packed):
        head_q, head_cot, head_lse, head_delta, head_lists, kv_index = packed
        head_keys = lax.dynamic_index_in_dim(key_blocks, kv_index, 0, keepdims=False)
        head_values = lax.dynamic_index_in_dim(value_blocks, kv_index, 0, keepdims=False)
        grad_query, own_gk, list_gk, own_gv, list_gv = sparse_terms(head_q, head_cot, head_keys, head_values, head_keys[head_lists], head_values[head_lists], head_lse, head_delta, head_lists, block_ids)
        grad_key = own_gk.at[head_lists].add(list_gk)
        grad_value = own_gv.at[head_lists].add(list_gv)
        return (grad_query.reshape(TOKENS, HD), grad_key.reshape(TOKENS, HD), grad_value.reshape(TOKENS, HD))
    q_heads = attn_q.reshape(n_blocks, BLK, Q_HEADS, HD).transpose(2, 0, 1, 3)
    cot_heads = attn_cot.reshape(n_blocks, BLK, Q_HEADS, HD).transpose(2, 0, 1, 3)
    kv_index = (jnp.arange(Q_HEADS) // group_size).astype(jnp.int32)
    grad_query, grad_key, grad_value = lax.map(per_head, (q_heads, cot_heads, attn_lse.reshape(Q_HEADS, n_blocks, BLK), attn_delta.reshape(Q_HEADS, n_blocks, BLK), block_lists, kv_index))
    attn_dq = grad_query.transpose(1, 0, 2).reshape(TOKENS, Q_HEADS * HD)
    attn_dk = grad_key.reshape(KV_HEADS, group_size, TOKENS, HD).sum(axis=1).transpose(1, 0, 2).reshape(TOKENS, KV_HEADS * HD)
    attn_dv = grad_value.reshape(KV_HEADS, group_size, TOKENS, HD).sum(axis=1).transpose(1, 0, 2).reshape(TOKENS, KV_HEADS * HD)
    return (attn_dq, attn_dk, attn_dv)

def reference(attn_q, attn_k, attn_v, attn_cot, attn_lse, attn_delta, block_lists, gdn_q, gdn_k, gdn_v, decay_logit, write_logit, decay_rate, write_scale, gdn_cot):
    attn_dq, attn_dk, attn_dv = attention_grads(attn_q, attn_k, attn_v, attn_cot, attn_lse, attn_delta, block_lists)
    raw_inputs = (gdn_q.astype(jnp.float32), gdn_k.astype(jnp.float32), gdn_v.astype(jnp.float32), decay_logit.astype(jnp.float32), write_logit.astype(jnp.float32))
    start_memory = jnp.zeros((GV_HEADS, GDIM, GDIM), jnp.float32)

    def run_layer(raw_values):
        return delta_forward(raw_values, start_memory, decay_rate, write_scale)[0]
    unused_out, pullback = jax.vjp(run_layer, raw_inputs)
    grads = pullback(gdn_cot.astype(jnp.float32))[0]
    return (attn_dq, attn_dk, attn_dv, grads[0], grads[1], grads[2], grads[3], grads[4])
```

```python
import jax
import jax.numpy as jnp
from jax import lax
from jax.sharding import PartitionSpec as P

Q_HEADS = 16
KV_HEADS = 2
HD = 256
GDIM = 128
BLK = 64
TOPK = 4
SPAN = 64


HIGHEST = lax.Precision.HIGHEST


def shifted(value, axis, step, backward):
    count = lax.axis_size(axis)
    if backward:
        pairs = [(i + step, i) for i in range(count - step)]
    else:
        pairs = [(i, i + step) for i in range(count - step)]
    return jax.tree.map(lambda part: lax.ppermute(part, axis, pairs), value)


def exclusive_scans(forward, backward, axis, join):
    count, mine = (lax.axis_size(axis), lax.axis_index(axis))
    step = 1
    while step < count:
        last = 2 * step >= count
        if last:
            got_f = (None, shifted(forward[1], axis, step, False))
            got_b = (None, shifted(backward[1], axis, step, True))
        else:
            got_f = shifted(forward, axis, step, False)
            got_b = shifted(backward, axis, step, True)
        new_f = join(got_f, forward, last)
        new_b = join(got_b, backward, last)
        forward = jax.tree.map(lambda n, o: jnp.where(mine >= step, n, o), new_f, forward)
        backward = jax.tree.map(lambda n, o: jnp.where(mine + step < count, n, o), new_b, backward)
        step *= 2
    return (shifted(forward[1], axis, 1, False), shifted(backward[1], axis, 1, True))


def unit_rows(matrix):
    return matrix / jnp.sqrt(jnp.sum(matrix * matrix, axis=-1, keepdims=True) + 1e-06)


def span_update(memory, packed):
    queries, keys_in, values_in, log_decay, write_gain = packed
    length = log_decay.shape[-1]
    cum_log = jnp.cumsum(log_decay, axis=-1)
    log_gap = cum_log[:, :, None] - cum_log[:, None, :]
    order_ids = jnp.arange(length)
    strict_low = order_ids[:, None] > order_ids[None, :]
    with_diag = order_ids[:, None] >= order_ids[None, :]
    decay_strict = jnp.where(strict_low, jnp.exp(jnp.where(strict_low, log_gap, 0.0)), 0.0)
    decay_upto = jnp.where(with_diag, jnp.exp(jnp.where(with_diag, log_gap, 0.0)), 0.0)
    key_gram = jnp.einsum("htd,hsd->hts", keys_in, keys_in, precision=HIGHEST)
    system = write_gain[:, :, None] * decay_strict * key_gram + jnp.eye(length, dtype=jnp.float32)
    decay_now = jnp.exp(cum_log)
    recalled = jnp.einsum("hvd,htd->htv", memory, keys_in, precision=HIGHEST)
    target = write_gain[:, :, None] * (values_in - decay_now[:, :, None] * recalled)
    written = lax.linalg.triangular_solve(
        system, target, left_side=True, lower=True, unit_diagonal=True
    )
    read_old = jnp.einsum("hvd,htd->htv", memory, queries, precision=HIGHEST)
    query_key = jnp.einsum("htd,hsd->hts", queries, keys_in, precision=HIGHEST)
    outputs = decay_now[:, :, None] * read_old + jnp.einsum(
        "hts,hsv->htv", decay_upto * query_key, written, precision=HIGHEST
    )
    tail_decay = jnp.exp(cum_log[:, -1:] - cum_log)
    memory_next = jnp.exp(cum_log[:, -1])[:, None, None] * memory + jnp.einsum(
        "hsv,hsd->hvd", written * tail_decay[:, :, None], keys_in, precision=HIGHEST
    )
    return (memory_next, outputs)


def delta_forward(raw_inputs, memory, rate_heads, scale_heads):
    query_raw, key_raw, value_raw, decay_in, write_in = raw_inputs
    n_tokens = query_raw.shape[0]
    key_heads = query_raw.shape[1] // GDIM
    value_heads = value_raw.shape[1] // GDIM
    ratio_heads = value_heads // key_heads
    n_spans = n_tokens // SPAN
    queries = jnp.repeat(
        unit_rows(query_raw.reshape(n_tokens, key_heads, GDIM)), ratio_heads, axis=1
    )
    keys_norm = jnp.repeat(
        unit_rows(key_raw.reshape(n_tokens, key_heads, GDIM)), ratio_heads, axis=1
    )
    values_in = value_raw.reshape(n_tokens, value_heads, GDIM)
    log_decay = -rate_heads[:, None] * jax.nn.softplus(decay_in)
    write_gain = scale_heads[:, None] * jax.nn.sigmoid(write_in)

    def blocks_of(tensor):
        return tensor.reshape(n_spans, SPAN, value_heads, GDIM).transpose(0, 2, 1, 3)

    def gates_of(tensor):
        return tensor.reshape(value_heads, n_spans, SPAN).transpose(1, 0, 2)

    memory_end, outputs = lax.scan(
        span_update,
        memory,
        (
            blocks_of(queries),
            blocks_of(keys_norm),
            blocks_of(values_in),
            gates_of(log_decay),
            gates_of(write_gain),
        ),
    )
    return (outputs.transpose(0, 2, 1, 3).reshape(n_tokens, value_heads * GDIM), memory_end)


def sparse_query_grad(
    q_blocks,
    cot_blocks,
    own_keys,
    own_values,
    listed_keys,
    listed_values,
    lse_rows,
    delta_rows,
    head_lists,
    block_ids,
):
    score_scale = HD ** (-0.5)
    position = jnp.arange(BLK)
    causal = position[:, None] >= position[None, :]
    slot_ids = jnp.arange(TOPK)
    repeated = jnp.any(
        (head_lists[:, :, None] == head_lists[:, None, :])
        & (slot_ids[:, None] > slot_ids[None, :]),
        axis=2,
    )
    usable = (head_lists < block_ids[:, None]) & jnp.logical_not(repeated)
    own_score = (
        jnp.einsum("bid,bjd->bij", q_blocks, own_keys, preferred_element_type=jnp.float32)
        * score_scale
    )
    list_score = (
        jnp.einsum("bid,btjd->bitj", q_blocks, listed_keys, preferred_element_type=jnp.float32)
        * score_scale
    )
    own_prob = jnp.where(causal[None], jnp.exp(own_score - lse_rows[:, :, None]), 0.0)
    list_prob = jnp.where(
        usable[:, None, :, None], jnp.exp(list_score - lse_rows[:, :, None, None]), 0.0
    )
    own_dprob = jnp.einsum(
        "bid,bjd->bij", cot_blocks, own_values, preferred_element_type=jnp.float32
    )
    list_dprob = jnp.einsum(
        "bid,btjd->bitj", cot_blocks, listed_values, preferred_element_type=jnp.float32
    )
    own_dscore = own_prob * (own_dprob - delta_rows[:, :, None])
    list_dscore = list_prob * (list_dprob - delta_rows[:, :, None, None])
    own_part = jnp.einsum(
        "bij,bjd->bid", own_dscore, own_keys.astype(jnp.float32), precision=HIGHEST
    )
    list_part = jnp.einsum(
        "bitj,btjd->bid", list_dscore, listed_keys.astype(jnp.float32), precision=HIGHEST
    )
    return (own_part + list_part) * score_scale


def compose_maps(earlier, later, last=False):
    shifted_part = jnp.einsum("hij,hjk->hik", earlier[1], later[0], precision=HIGHEST) + later[1]
    if last:
        return (later[0], shifted_part)
    product = jnp.einsum("hij,hjk->hik", earlier[0], later[0], precision=HIGHEST)
    return (product, shifted_part)


def on_device(
    attn_q,
    attn_k,
    attn_v,
    attn_cot,
    attn_lse,
    attn_delta,
    block_lists,
    gdn_q,
    gdn_k,
    gdn_v,
    decay_logit,
    write_logit,
    decay_rate,
    write_scale,
    gdn_cot,
):
    score_scale = HD ** (-0.5)
    head_index = lax.axis_index("head")
    ctx_index = lax.axis_index("ctx")
    tok_rows = attn_q.shape[0]
    local_heads = attn_q.shape[1] // HD
    blocks_here = tok_rows // BLK
    kv_group = head_index * local_heads // (Q_HEADS // KV_HEADS)
    own_keys = lax.dynamic_index_in_dim(
        attn_k.reshape(tok_rows, KV_HEADS, HD), kv_group, 1, keepdims=False
    )
    own_values = lax.dynamic_index_in_dim(
        attn_v.reshape(tok_rows, KV_HEADS, HD), kv_group, 1, keepdims=False
    )
    row_base = ctx_index * tok_rows
    first_block = ctx_index * blocks_here
    key_block_ids = first_block + jnp.arange(blocks_here, dtype=jnp.int32)
    member = jnp.any(block_lists[:, :, :, None] == key_block_ids[None, None, None, :], axis=2)
    member_rows = jnp.repeat(jnp.repeat(member, BLK, axis=1), BLK, axis=2)
    key_pos = row_base + jnp.arange(tok_rows, dtype=jnp.int32)
    key_block = key_pos // BLK
    packed = jnp.concatenate([own_keys, own_values, attn_q, attn_cot], axis=1)
    gathered = lax.all_gather(packed, "ctx", axis=0, tiled=True)
    keys_whole = gathered[:, :HD]
    values_whole = gathered[:, HD : 2 * HD]
    lists_own = lax.dynamic_slice_in_dim(block_lists, first_block, blocks_here, 1)
    lse_own = lax.dynamic_slice_in_dim(attn_lse, row_base, tok_rows, 1).reshape(
        local_heads, blocks_here, BLK
    )
    delta_own = lax.dynamic_slice_in_dim(attn_delta, row_base, tok_rows, 1).reshape(
        local_heads, blocks_here, BLK
    )
    q_blocks = attn_q.reshape(blocks_here, BLK, local_heads, HD).transpose(2, 0, 1, 3)
    cot_blocks = attn_cot.reshape(blocks_here, BLK, local_heads, HD).transpose(2, 0, 1, 3)
    listed_keys = keys_whole.reshape(-1, BLK, HD)[lists_own]
    listed_values = values_whole.reshape(-1, BLK, HD)[lists_own]
    grad_blocks = jax.vmap(sparse_query_grad, in_axes=(0, 0, None, None, 0, 0, 0, 0, 0, None))(
        q_blocks,
        cot_blocks,
        own_keys.reshape(blocks_here, BLK, HD),
        own_values.reshape(blocks_here, BLK, HD),
        listed_keys,
        listed_values,
        lse_own,
        delta_own,
        lists_own,
        key_block_ids,
    )
    grad_q = grad_blocks.transpose(1, 2, 0, 3).reshape(tok_rows, local_heads * HD)
    width = local_heads * HD
    n_rows = gathered.shape[0]
    queries = gathered[:, 2 * HD : 2 * HD + width].reshape(n_rows, local_heads, HD)
    cotangent = gathered[:, 2 * HD + width :].reshape(n_rows, local_heads, HD)
    row_pos = jnp.arange(n_rows, dtype=jnp.int32)
    row_block = row_pos // BLK
    own_pair = (row_block[:, None] == key_block[None, :]) & (row_pos[:, None] >= key_pos[None, :])
    listed_pair = member_rows & (key_block[None, :] < row_block[:, None])[None]
    allowed = own_pair[None] | listed_pair
    scores = (
        jnp.einsum("nhd,kd->hnk", queries, own_keys, preferred_element_type=jnp.float32)
        * score_scale
    )
    prob_full = jnp.where(allowed, jnp.exp(scores - attn_lse[:, :, None]), 0.0)
    dprobs = jnp.einsum("nhd,kd->hnk", cotangent, own_values, preferred_element_type=jnp.float32)
    dscores = prob_full * (dprobs - attn_delta[:, :, None])
    grad_value = jnp.einsum(
        "hnk,nhd->kd", prob_full, cotangent.astype(jnp.float32), precision=HIGHEST
    )
    grad_key = (
        jnp.einsum("hnk,nhd->kd", dscores, queries.astype(jnp.float32), precision=HIGHEST)
        * score_scale
    )
    slot_mask = (jnp.arange(KV_HEADS) == kv_group)[None, :, None]
    key_slots = jnp.where(slot_mask, grad_key[:, None, :], 0.0).reshape(tok_rows, KV_HEADS * HD)
    value_slots = jnp.where(slot_mask, grad_value[:, None, :], 0.0).reshape(tok_rows, KV_HEADS * HD)
    attn_dk, attn_dv = lax.psum((key_slots, value_slots), "head")
    raw_inputs = (
        gdn_q.astype(jnp.float32),
        gdn_k.astype(jnp.float32),
        gdn_v.astype(jnp.float32),
        decay_logit,
        write_logit,
    )
    value_heads = gdn_v.shape[1] // GDIM
    zero_memory = jnp.zeros((value_heads, GDIM, GDIM), jnp.float32)
    unit_memory = jnp.broadcast_to(jnp.eye(GDIM, dtype=jnp.float32), zero_memory.shape)

    def local_run(raw_values, memory):
        return delta_forward(raw_values, memory, decay_rate, write_scale)

    silent_inputs = (
        raw_inputs[0],
        raw_inputs[1],
        jnp.zeros_like(raw_inputs[2]),
        raw_inputs[3],
        raw_inputs[4],
    )
    transition = local_run(silent_inputs, unit_memory)[1]
    outputs_zero, pull_zero = jax.vjp(local_run, raw_inputs, zero_memory)
    written_end = outputs_zero[1]
    cot_full = gdn_cot.astype(jnp.float32)
    local_grad = pull_zero((cot_full, zero_memory))[1]
    memory_in, memory_grad = exclusive_scans(
        (transition, written_end),
        (jnp.swapaxes(transition, 1, 2), local_grad),
        "ctx",
        compose_maps,
    )
    unused_out, pull_final = jax.vjp(local_run, raw_inputs, memory_in)
    grads = pull_final((cot_full, memory_grad))[0]
    return (grad_q, attn_dk, attn_dv, grads[0], grads[1], grads[2], grads[3], grads[4])


def solution(mesh):
    return jax.shard_map(
        on_device,
        mesh=mesh,
        in_specs=(
            P("ctx", "head"),
            P("ctx", None),
            P("ctx", None),
            P("ctx", "head"),
            P("head", None),
            P("head", None),
            P("head", None, None),
            P("ctx", "head"),
            P("ctx", "head"),
            P("ctx", "head"),
            P("head", "ctx"),
            P("head", "ctx"),
            P("head"),
            P("head"),
            P("ctx", "head"),
        ),
        out_specs=(
            P("ctx", "head"),
            P("ctx", None),
            P("ctx", None),
            P("ctx", "head"),
            P("ctx", "head"),
            P("ctx", "head"),
            P("head", "ctx"),
            P("head", "ctx"),
        ),
        check_vma=False,
    )
```

```python
import jax
import jax.numpy as jnp
from jax import lax
from jax.sharding import PartitionSpec as P

Q_HEADS = 16
KV_HEADS = 2
HD = 256
GDIM = 128
BLK = 64
TOPK = 4
SPAN = 64


HIGHEST = lax.Precision.HIGHEST


def shifted(value, axis, step, backward):
    count = lax.axis_size(axis)
    if backward:
        pairs = [(i + step, i) for i in range(count - step)]
    else:
        pairs = [(i, i + step) for i in range(count - step)]
    return jax.tree.map(lambda part: lax.ppermute(part, axis, pairs), value)


def exclusive_scans(forward, backward, axis, join, hold):
    count, mine = (lax.axis_size(axis), lax.axis_index(axis))
    step = 1
    while step < count:
        last = 2 * step >= count
        if last:
            got_f = (None, shifted(forward[1], axis, step, False))
            got_b = (None, shifted(backward[1], axis, step, True))
        else:
            got_f = shifted(forward, axis, step, False)
            got_b = shifted(backward, axis, step, True)
        if step == 1:
            got_f, got_b, hold = lax.optimization_barrier((got_f, got_b, hold))
        new_f = join(got_f, forward, last)
        new_b = join(got_b, backward, last)
        forward = jax.tree.map(lambda n, o: jnp.where(mine >= step, n, o), new_f, forward)
        backward = jax.tree.map(lambda n, o: jnp.where(mine + step < count, n, o), new_b, backward)
        step *= 2
    return (shifted(forward[1], axis, 1, False), shifted(backward[1], axis, 1, True), hold)


def butterfly_sum(value, axis, start, stop):
    count = lax.axis_size(axis)
    dist = start
    while dist < stop:
        pairs = [(i, i ^ dist) for i in range(count)]
        got = jax.tree.map(lambda part: lax.ppermute(part, axis, pairs), value)
        value = jax.tree.map(jnp.add, value, got)
        dist *= 2
    return value


def unit_rows(matrix):
    return matrix / jnp.sqrt(jnp.sum(matrix * matrix, axis=-1, keepdims=True) + 1e-06)


def span_update(memory, packed):
    queries, keys_in, values_in, log_decay, write_gain = packed
    length = log_decay.shape[-1]
    cum_log = jnp.cumsum(log_decay, axis=-1)
    log_gap = cum_log[:, :, None] - cum_log[:, None, :]
    order_ids = jnp.arange(length)
    strict_low = order_ids[:, None] > order_ids[None, :]
    with_diag = order_ids[:, None] >= order_ids[None, :]
    decay_strict = jnp.where(strict_low, jnp.exp(jnp.where(strict_low, log_gap, 0.0)), 0.0)
    decay_upto = jnp.where(with_diag, jnp.exp(jnp.where(with_diag, log_gap, 0.0)), 0.0)
    key_gram = jnp.einsum("htd,hsd->hts", keys_in, keys_in, precision=HIGHEST)
    system = write_gain[:, :, None] * decay_strict * key_gram + jnp.eye(length, dtype=jnp.float32)
    decay_now = jnp.exp(cum_log)
    recalled = jnp.einsum("hvd,htd->htv", memory, keys_in, precision=HIGHEST)
    target = write_gain[:, :, None] * (values_in - decay_now[:, :, None] * recalled)
    written = lax.linalg.triangular_solve(
        system, target, left_side=True, lower=True, unit_diagonal=True
    )
    read_old = jnp.einsum("hvd,htd->htv", memory, queries, precision=HIGHEST)
    query_key = jnp.einsum("htd,hsd->hts", queries, keys_in, precision=HIGHEST)
    outputs = decay_now[:, :, None] * read_old + jnp.einsum(
        "hts,hsv->htv", decay_upto * query_key, written, precision=HIGHEST
    )
    tail_decay = jnp.exp(cum_log[:, -1:] - cum_log)
    memory_next = jnp.exp(cum_log[:, -1])[:, None, None] * memory + jnp.einsum(
        "hsv,hsd->hvd", written * tail_decay[:, :, None], keys_in, precision=HIGHEST
    )
    return (memory_next, outputs)


def delta_forward(raw_inputs, memory, rate_heads, scale_heads):
    query_raw, key_raw, value_raw, decay_in, write_in = raw_inputs
    n_tokens = query_raw.shape[0]
    key_heads = query_raw.shape[1] // GDIM
    value_heads = value_raw.shape[1] // GDIM
    ratio_heads = value_heads // key_heads
    n_spans = n_tokens // SPAN
    queries = jnp.repeat(
        unit_rows(query_raw.reshape(n_tokens, key_heads, GDIM)), ratio_heads, axis=1
    )
    keys_norm = jnp.repeat(
        unit_rows(key_raw.reshape(n_tokens, key_heads, GDIM)), ratio_heads, axis=1
    )
    values_in = value_raw.reshape(n_tokens, value_heads, GDIM)
    log_decay = -rate_heads[:, None] * jax.nn.softplus(decay_in)
    write_gain = scale_heads[:, None] * jax.nn.sigmoid(write_in)

    def blocks_of(tensor):
        return tensor.reshape(n_spans, SPAN, value_heads, GDIM).transpose(0, 2, 1, 3)

    def gates_of(tensor):
        return tensor.reshape(value_heads, n_spans, SPAN).transpose(1, 0, 2)

    memory_end, outputs = lax.scan(
        span_update,
        memory,
        (
            blocks_of(queries),
            blocks_of(keys_norm),
            blocks_of(values_in),
            gates_of(log_decay),
            gates_of(write_gain),
        ),
    )
    return (outputs.transpose(0, 2, 1, 3).reshape(n_tokens, value_heads * GDIM), memory_end)


def sparse_query_grad(
    q_blocks,
    cot_blocks,
    own_keys,
    own_values,
    listed_keys,
    listed_values,
    lse_rows,
    delta_rows,
    head_lists,
    block_ids,
):
    score_scale = HD ** (-0.5)
    position = jnp.arange(BLK)
    causal = position[:, None] >= position[None, :]
    slot_ids = jnp.arange(TOPK)
    repeated = jnp.any(
        (head_lists[:, :, None] == head_lists[:, None, :])
        & (slot_ids[:, None] > slot_ids[None, :]),
        axis=2,
    )
    usable = (head_lists < block_ids[:, None]) & jnp.logical_not(repeated)
    own_score = (
        jnp.einsum("bid,bjd->bij", q_blocks, own_keys, preferred_element_type=jnp.float32)
        * score_scale
    )
    list_score = (
        jnp.einsum("bid,btjd->bitj", q_blocks, listed_keys, preferred_element_type=jnp.float32)
        * score_scale
    )
    own_prob = jnp.where(causal[None], jnp.exp(own_score - lse_rows[:, :, None]), 0.0)
    list_prob = jnp.where(
        usable[:, None, :, None], jnp.exp(list_score - lse_rows[:, :, None, None]), 0.0
    )
    own_dprob = jnp.einsum(
        "bid,bjd->bij", cot_blocks, own_values, preferred_element_type=jnp.float32
    )
    list_dprob = jnp.einsum(
        "bid,btjd->bitj", cot_blocks, listed_values, preferred_element_type=jnp.float32
    )
    own_dscore = own_prob * (own_dprob - delta_rows[:, :, None])
    list_dscore = list_prob * (list_dprob - delta_rows[:, :, None, None])
    own_part = jnp.einsum(
        "bij,bjd->bid", own_dscore, own_keys.astype(jnp.float32), precision=HIGHEST
    )
    list_part = jnp.einsum(
        "bitj,btjd->bid", list_dscore, listed_keys.astype(jnp.float32), precision=HIGHEST
    )
    return (own_part + list_part) * score_scale


def compose_maps(earlier, later, last=False):
    shifted_part = jnp.einsum("hij,hjk->hik", earlier[1], later[0], precision=HIGHEST) + later[1]
    if last:
        return (later[0], shifted_part)
    product = jnp.einsum("hij,hjk->hik", earlier[0], later[0], precision=HIGHEST)
    return (product, shifted_part)


def on_device(
    attn_q,
    attn_k,
    attn_v,
    attn_cot,
    attn_lse,
    attn_delta,
    block_lists,
    gdn_q,
    gdn_k,
    gdn_v,
    decay_logit,
    write_logit,
    decay_rate,
    write_scale,
    gdn_cot,
):
    score_scale = HD ** (-0.5)
    head_index = lax.axis_index("head")
    ctx_index = lax.axis_index("ctx")
    tok_rows = attn_q.shape[0]
    local_heads = attn_q.shape[1] // HD
    blocks_here = tok_rows // BLK
    kv_group = head_index * local_heads // (Q_HEADS // KV_HEADS)
    own_keys = lax.dynamic_index_in_dim(
        attn_k.reshape(tok_rows, KV_HEADS, HD), kv_group, 1, keepdims=False
    )
    own_values = lax.dynamic_index_in_dim(
        attn_v.reshape(tok_rows, KV_HEADS, HD), kv_group, 1, keepdims=False
    )
    row_base = ctx_index * tok_rows
    first_block = ctx_index * blocks_here
    key_block_ids = first_block + jnp.arange(blocks_here, dtype=jnp.int32)
    member = jnp.any(block_lists[:, :, :, None] == key_block_ids[None, None, None, :], axis=2)
    member_rows = jnp.repeat(jnp.repeat(member, BLK, axis=1), BLK, axis=2)
    key_pos = row_base + jnp.arange(tok_rows, dtype=jnp.int32)
    key_block = key_pos // BLK
    packed = jnp.concatenate([own_keys, own_values, attn_q, attn_cot], axis=1)
    gathered = lax.all_gather(packed, "ctx", axis=0, tiled=True)
    keys_whole = gathered[:, :HD]
    values_whole = gathered[:, HD : 2 * HD]
    lists_own = lax.dynamic_slice_in_dim(block_lists, first_block, blocks_here, 1)
    lse_own = lax.dynamic_slice_in_dim(attn_lse, row_base, tok_rows, 1).reshape(
        local_heads, blocks_here, BLK
    )
    delta_own = lax.dynamic_slice_in_dim(attn_delta, row_base, tok_rows, 1).reshape(
        local_heads, blocks_here, BLK
    )
    q_blocks = attn_q.reshape(blocks_here, BLK, local_heads, HD).transpose(2, 0, 1, 3)
    cot_blocks = attn_cot.reshape(blocks_here, BLK, local_heads, HD).transpose(2, 0, 1, 3)
    listed_keys = keys_whole.reshape(-1, BLK, HD)[lists_own]
    listed_values = values_whole.reshape(-1, BLK, HD)[lists_own]
    grad_blocks = jax.vmap(sparse_query_grad, in_axes=(0, 0, None, None, 0, 0, 0, 0, 0, None))(
        q_blocks,
        cot_blocks,
        own_keys.reshape(blocks_here, BLK, HD),
        own_values.reshape(blocks_here, BLK, HD),
        listed_keys,
        listed_values,
        lse_own,
        delta_own,
        lists_own,
        key_block_ids,
    )
    grad_q = grad_blocks.transpose(1, 2, 0, 3).reshape(tok_rows, local_heads * HD)
    width = local_heads * HD
    n_rows = gathered.shape[0]
    queries = gathered[:, 2 * HD : 2 * HD + width].reshape(n_rows, local_heads, HD)
    cotangent = gathered[:, 2 * HD + width :].reshape(n_rows, local_heads, HD)
    row_pos = jnp.arange(n_rows, dtype=jnp.int32)
    row_block = row_pos // BLK
    own_pair = (row_block[:, None] == key_block[None, :]) & (row_pos[:, None] >= key_pos[None, :])
    listed_pair = member_rows & (key_block[None, :] < row_block[:, None])[None]
    allowed = own_pair[None] | listed_pair
    scores = (
        jnp.einsum("nhd,kd->hnk", queries, own_keys, preferred_element_type=jnp.float32)
        * score_scale
    )
    prob_full = jnp.where(allowed, jnp.exp(scores - attn_lse[:, :, None]), 0.0)
    dprobs = jnp.einsum("nhd,kd->hnk", cotangent, own_values, preferred_element_type=jnp.float32)
    dscores = prob_full * (dprobs - attn_delta[:, :, None])
    grad_value = jnp.einsum(
        "hnk,nhd->kd", prob_full, cotangent.astype(jnp.float32), precision=HIGHEST
    )
    grad_key = (
        jnp.einsum("hnk,nhd->kd", dscores, queries.astype(jnp.float32), precision=HIGHEST)
        * score_scale
    )
    group_devices = max(1, (Q_HEADS // KV_HEADS) // local_heads)
    raw_inputs = (
        gdn_q.astype(jnp.float32),
        gdn_k.astype(jnp.float32),
        gdn_v.astype(jnp.float32),
        decay_logit,
        write_logit,
    )
    value_heads = gdn_v.shape[1] // GDIM
    zero_memory = jnp.zeros((value_heads, GDIM, GDIM), jnp.float32)
    unit_memory = jnp.broadcast_to(jnp.eye(GDIM, dtype=jnp.float32), zero_memory.shape)

    def local_run(raw_values, memory):
        return delta_forward(raw_values, memory, decay_rate, write_scale)

    silent_inputs = (
        raw_inputs[0],
        raw_inputs[1],
        jnp.zeros_like(raw_inputs[2]),
        raw_inputs[3],
        raw_inputs[4],
    )
    transition = local_run(silent_inputs, unit_memory)[1]
    outputs_zero, pull_zero = jax.vjp(local_run, raw_inputs, zero_memory)
    written_end = outputs_zero[1]
    cot_full = gdn_cot.astype(jnp.float32)
    local_grad = pull_zero((cot_full, zero_memory))[1]
    memory_in, memory_grad, (grad_q, group_sums) = exclusive_scans(
        (transition, written_end),
        (jnp.swapaxes(transition, 1, 2), local_grad),
        "ctx",
        compose_maps,
        (grad_q, (grad_key, grad_value)),
    )
    group_sums = butterfly_sum(group_sums, "head", 1, group_devices)
    slot_mask = (jnp.arange(KV_HEADS) == kv_group)[None, :, None]
    key_slots = jnp.where(slot_mask, group_sums[0][:, None, :], 0.0).reshape(tok_rows, KV_HEADS * HD)
    value_slots = jnp.where(slot_mask, group_sums[1][:, None, :], 0.0).reshape(
        tok_rows, KV_HEADS * HD
    )
    attn_dk, attn_dv = butterfly_sum(
        (key_slots, value_slots), "head", group_devices, lax.axis_size("head")
    )
    memory_in, memory_grad, grad_q, attn_dk, attn_dv = lax.optimization_barrier(
        (memory_in, memory_grad, grad_q, attn_dk, attn_dv)
    )
    unused_out, pull_final = jax.vjp(local_run, raw_inputs, memory_in)
    grads = pull_final((cot_full, memory_grad))[0]
    return (grad_q, attn_dk, attn_dv, grads[0], grads[1], grads[2], grads[3], grads[4])


def solution(mesh):
    return jax.shard_map(
        on_device,
        mesh=mesh,
        in_specs=(
            P("ctx", "head"),
            P("ctx", None),
            P("ctx", None),
            P("ctx", "head"),
            P("head", None),
            P("head", None),
            P("head", None, None),
            P("ctx", "head"),
            P("ctx", "head"),
            P("ctx", "head"),
            P("head", "ctx"),
            P("head", "ctx"),
            P("head"),
            P("head"),
            P("ctx", "head"),
        ),
        out_specs=(
            P("ctx", "head"),
            P("ctx", None),
            P("ctx", None),
            P("ctx", "head"),
            P("ctx", "head"),
            P("ctx", "head"),
            P("head", "ctx"),
            P("head", "ctx"),
        ),
        check_vma=False,
    )
```

```python
import jax
import jax.numpy as jnp
from jax import lax
from jax.sharding import PartitionSpec as P

Q_HEADS = 16
KV_HEADS = 2
HD = 256
GDIM = 128
BLK = 64
TOPK = 4
SPAN = 64


HIGHEST = lax.Precision.HIGHEST


def shifted(value, axis, step, backward):
    count = lax.axis_size(axis)
    if backward:
        pairs = [(i + step, i) for i in range(count - step)]
    else:
        pairs = [(i, i + step) for i in range(count - step)]
    return jax.tree.map(lambda part: lax.ppermute(part, axis, pairs), value)


def exclusive_scans(forward, backward, axis, join, hold):
    count, mine = (lax.axis_size(axis), lax.axis_index(axis))
    step = 1
    while step < count:
        last = 2 * step >= count
        if last:
            got_f = (None, shifted(forward[1], axis, step, False))
            got_b = (None, shifted(backward[1], axis, step, True))
        else:
            got_f = shifted(forward, axis, step, False)
            got_b = shifted(backward, axis, step, True)
        if step == 1:
            got_f, got_b, hold = lax.optimization_barrier((got_f, got_b, hold))
        new_f = join(got_f, forward, last)
        new_b = join(got_b, backward, last)
        forward = jax.tree.map(lambda n, o: jnp.where(mine >= step, n, o), new_f, forward)
        backward = jax.tree.map(lambda n, o: jnp.where(mine + step < count, n, o), new_b, backward)
        step *= 2
    return (shifted(forward[1], axis, 1, False), shifted(backward[1], axis, 1, True), hold)


def butterfly_sum(value, axis, start, stop):
    count = lax.axis_size(axis)
    dist = start
    while dist < stop:
        pairs = [(i, i ^ dist) for i in range(count)]
        got = jax.tree.map(lambda part: lax.ppermute(part, axis, pairs), value)
        value = jax.tree.map(jnp.add, value, got)
        dist *= 2
    return value


def unit_rows(matrix):
    return matrix / jnp.sqrt(jnp.sum(matrix * matrix, axis=-1, keepdims=True) + 1e-06)


def pair_blocks(matrix, size):
    heads, n = (matrix.shape[0], matrix.shape[1] // (2 * size))
    tiles = matrix.reshape(heads, n, 2, size, n, 2, size)[:, :, 1, :, :, 0, :]
    same = (jnp.arange(n)[:, None] == jnp.arange(n)[None, :])[None, :, None, :, None]
    return jnp.sum(jnp.where(same, tiles, 0.0), axis=3)


def unit_lower_inverse(system):
    heads, n = (system.shape[0], system.shape[1])
    blocks = jnp.ones((heads, n, 1, 1), jnp.float32)
    size = 1
    while size < n:
        upper_inv = blocks[:, 0::2]
        lower_inv = blocks[:, 1::2]
        coupling = pair_blocks(system, size)
        mixed = -jnp.einsum(
            "hkij,hkjl->hkil",
            lower_inv,
            jnp.einsum("hkij,hkjl->hkil", coupling, upper_inv, precision=HIGHEST),
            precision=HIGHEST,
        )
        top = jnp.concatenate([upper_inv, jnp.zeros_like(upper_inv)], axis=3)
        bottom = jnp.concatenate([mixed, lower_inv], axis=3)
        blocks = jnp.concatenate([top, bottom], axis=2)
        size *= 2
    return blocks[:, 0]


@jax.custom_vjp
def unit_lower_solve(system, target):
    return jnp.einsum("hts,hsv->htv", unit_lower_inverse(system), target, precision=HIGHEST)


def unit_lower_solve_fwd(system, target):
    inverse = unit_lower_inverse(system)
    solved = jnp.einsum("hts,hsv->htv", inverse, target, precision=HIGHEST)
    return (solved, (inverse, solved))


def unit_lower_solve_bwd(saved, grad_solved):
    inverse, solved = saved
    grad_target = jnp.einsum("hst,hsv->htv", inverse, grad_solved, precision=HIGHEST)
    length = inverse.shape[-1]
    strict = jnp.arange(length)[:, None] > jnp.arange(length)[None, :]
    grad_system = jnp.where(
        strict, -jnp.einsum("htv,hsv->hts", grad_target, solved, precision=HIGHEST), 0.0
    )
    return (grad_system, grad_target)


unit_lower_solve.defvjp(unit_lower_solve_fwd, unit_lower_solve_bwd)


def span_update(memory, packed):
    queries, keys_in, values_in, log_decay, write_gain = packed
    length = log_decay.shape[-1]
    cum_log = jnp.cumsum(log_decay, axis=-1)
    log_gap = cum_log[:, :, None] - cum_log[:, None, :]
    order_ids = jnp.arange(length)
    strict_low = order_ids[:, None] > order_ids[None, :]
    with_diag = order_ids[:, None] >= order_ids[None, :]
    decay_strict = jnp.where(strict_low, jnp.exp(jnp.where(strict_low, log_gap, 0.0)), 0.0)
    decay_upto = jnp.where(with_diag, jnp.exp(jnp.where(with_diag, log_gap, 0.0)), 0.0)
    key_gram = jnp.einsum("htd,hsd->hts", keys_in, keys_in, precision=HIGHEST)
    system = write_gain[:, :, None] * decay_strict * key_gram + jnp.eye(length, dtype=jnp.float32)
    decay_now = jnp.exp(cum_log)
    recalled = jnp.einsum("hvd,htd->htv", memory, keys_in, precision=HIGHEST)
    target = write_gain[:, :, None] * (values_in - decay_now[:, :, None] * recalled)
    written = unit_lower_solve(system, target)
    read_old = jnp.einsum("hvd,htd->htv", memory, queries, precision=HIGHEST)
    query_key = jnp.einsum("htd,hsd->hts", queries, keys_in, precision=HIGHEST)
    outputs = decay_now[:, :, None] * read_old + jnp.einsum(
        "hts,hsv->htv", decay_upto * query_key, written, precision=HIGHEST
    )
    tail_decay = jnp.exp(cum_log[:, -1:] - cum_log)
    memory_next = jnp.exp(cum_log[:, -1])[:, None, None] * memory + jnp.einsum(
        "hsv,hsd->hvd", written * tail_decay[:, :, None], keys_in, precision=HIGHEST
    )
    return (memory_next, outputs)


def delta_forward(raw_inputs, memory, rate_heads, scale_heads):
    query_raw, key_raw, value_raw, decay_in, write_in = raw_inputs
    n_tokens = query_raw.shape[0]
    key_heads = query_raw.shape[1] // GDIM
    value_heads = value_raw.shape[1] // GDIM
    ratio_heads = value_heads // key_heads
    n_spans = n_tokens // SPAN
    queries = jnp.repeat(
        unit_rows(query_raw.reshape(n_tokens, key_heads, GDIM)), ratio_heads, axis=1
    )
    keys_norm = jnp.repeat(
        unit_rows(key_raw.reshape(n_tokens, key_heads, GDIM)), ratio_heads, axis=1
    )
    values_in = value_raw.reshape(n_tokens, value_heads, GDIM)
    log_decay = -rate_heads[:, None] * jax.nn.softplus(decay_in)
    write_gain = scale_heads[:, None] * jax.nn.sigmoid(write_in)

    def blocks_of(tensor):
        return tensor.reshape(n_spans, SPAN, value_heads, GDIM).transpose(0, 2, 1, 3)

    def gates_of(tensor):
        return tensor.reshape(value_heads, n_spans, SPAN).transpose(1, 0, 2)

    memory_end, outputs = lax.scan(
        span_update,
        memory,
        (
            blocks_of(queries),
            blocks_of(keys_norm),
            blocks_of(values_in),
            gates_of(log_decay),
            gates_of(write_gain),
        ),
    )
    return (outputs.transpose(0, 2, 1, 3).reshape(n_tokens, value_heads * GDIM), memory_end)


def sparse_query_grad(
    q_blocks,
    cot_blocks,
    own_keys,
    own_values,
    listed_keys,
    listed_values,
    lse_rows,
    delta_rows,
    head_lists,
    block_ids,
):
    score_scale = HD ** (-0.5)
    position = jnp.arange(BLK)
    causal = position[:, None] >= position[None, :]
    slot_ids = jnp.arange(TOPK)
    repeated = jnp.any(
        (head_lists[:, :, None] == head_lists[:, None, :])
        & (slot_ids[:, None] > slot_ids[None, :]),
        axis=2,
    )
    usable = (head_lists < block_ids[:, None]) & jnp.logical_not(repeated)
    own_score = (
        jnp.einsum("bid,bjd->bij", q_blocks, own_keys, preferred_element_type=jnp.float32)
        * score_scale
    )
    list_score = (
        jnp.einsum("bid,btjd->bitj", q_blocks, listed_keys, preferred_element_type=jnp.float32)
        * score_scale
    )
    own_prob = jnp.where(causal[None], jnp.exp(own_score - lse_rows[:, :, None]), 0.0)
    list_prob = jnp.where(
        usable[:, None, :, None], jnp.exp(list_score - lse_rows[:, :, None, None]), 0.0
    )
    own_dprob = jnp.einsum(
        "bid,bjd->bij", cot_blocks, own_values, preferred_element_type=jnp.float32
    )
    list_dprob = jnp.einsum(
        "bid,btjd->bitj", cot_blocks, listed_values, preferred_element_type=jnp.float32
    )
    own_dscore = own_prob * (own_dprob - delta_rows[:, :, None])
    list_dscore = list_prob * (list_dprob - delta_rows[:, :, None, None])
    own_part = jnp.einsum(
        "bij,bjd->bid", own_dscore, own_keys.astype(jnp.float32), precision=HIGHEST
    )
    list_part = jnp.einsum(
        "bitj,btjd->bid", list_dscore, listed_keys.astype(jnp.float32), precision=HIGHEST
    )
    return (own_part + list_part) * score_scale


def compose_maps(earlier, later, last=False):
    shifted_part = jnp.einsum("hij,hjk->hik", earlier[1], later[0], precision=HIGHEST) + later[1]
    if last:
        return (later[0], shifted_part)
    product = jnp.einsum("hij,hjk->hik", earlier[0], later[0], precision=HIGHEST)
    return (product, shifted_part)


def on_device(
    attn_q,
    attn_k,
    attn_v,
    attn_cot,
    attn_lse,
    attn_delta,
    block_lists,
    gdn_q,
    gdn_k,
    gdn_v,
    decay_logit,
    write_logit,
    decay_rate,
    write_scale,
    gdn_cot,
):
    score_scale = HD ** (-0.5)
    head_index = lax.axis_index("head")
    ctx_index = lax.axis_index("ctx")
    tok_rows = attn_q.shape[0]
    local_heads = attn_q.shape[1] // HD
    blocks_here = tok_rows // BLK
    kv_group = head_index * local_heads // (Q_HEADS // KV_HEADS)
    own_keys = lax.dynamic_index_in_dim(
        attn_k.reshape(tok_rows, KV_HEADS, HD), kv_group, 1, keepdims=False
    )
    own_values = lax.dynamic_index_in_dim(
        attn_v.reshape(tok_rows, KV_HEADS, HD), kv_group, 1, keepdims=False
    )
    row_base = ctx_index * tok_rows
    first_block = ctx_index * blocks_here
    key_block_ids = first_block + jnp.arange(blocks_here, dtype=jnp.int32)
    member = jnp.any(block_lists[:, :, :, None] == key_block_ids[None, None, None, :], axis=2)
    member_rows = jnp.repeat(jnp.repeat(member, BLK, axis=1), BLK, axis=2)
    key_pos = row_base + jnp.arange(tok_rows, dtype=jnp.int32)
    key_block = key_pos // BLK
    packed = jnp.concatenate([own_keys, own_values, attn_q, attn_cot], axis=1)
    gathered = lax.all_gather(packed, "ctx", axis=0, tiled=True)
    keys_whole = gathered[:, :HD]
    values_whole = gathered[:, HD : 2 * HD]
    lists_own = lax.dynamic_slice_in_dim(block_lists, first_block, blocks_here, 1)
    lse_own = lax.dynamic_slice_in_dim(attn_lse, row_base, tok_rows, 1).reshape(
        local_heads, blocks_here, BLK
    )
    delta_own = lax.dynamic_slice_in_dim(attn_delta, row_base, tok_rows, 1).reshape(
        local_heads, blocks_here, BLK
    )
    q_blocks = attn_q.reshape(blocks_here, BLK, local_heads, HD).transpose(2, 0, 1, 3)
    cot_blocks = attn_cot.reshape(blocks_here, BLK, local_heads, HD).transpose(2, 0, 1, 3)
    listed_keys = keys_whole.reshape(-1, BLK, HD)[lists_own]
    listed_values = values_whole.reshape(-1, BLK, HD)[lists_own]
    grad_blocks = jax.vmap(sparse_query_grad, in_axes=(0, 0, None, None, 0, 0, 0, 0, 0, None))(
        q_blocks,
        cot_blocks,
        own_keys.reshape(blocks_here, BLK, HD),
        own_values.reshape(blocks_here, BLK, HD),
        listed_keys,
        listed_values,
        lse_own,
        delta_own,
        lists_own,
        key_block_ids,
    )
    grad_q = grad_blocks.transpose(1, 2, 0, 3).reshape(tok_rows, local_heads * HD)
    width = local_heads * HD
    n_rows = gathered.shape[0]
    queries = gathered[:, 2 * HD : 2 * HD + width].reshape(n_rows, local_heads, HD)
    cotangent = gathered[:, 2 * HD + width :].reshape(n_rows, local_heads, HD)
    row_pos = jnp.arange(n_rows, dtype=jnp.int32)
    row_block = row_pos // BLK
    own_pair = (row_block[:, None] == key_block[None, :]) & (row_pos[:, None] >= key_pos[None, :])
    listed_pair = member_rows & (key_block[None, :] < row_block[:, None])[None]
    allowed = own_pair[None] | listed_pair
    scores = (
        jnp.einsum("nhd,kd->hnk", queries, own_keys, preferred_element_type=jnp.float32)
        * score_scale
    )
    prob_full = jnp.where(allowed, jnp.exp(scores - attn_lse[:, :, None]), 0.0)
    dprobs = jnp.einsum("nhd,kd->hnk", cotangent, own_values, preferred_element_type=jnp.float32)
    dscores = prob_full * (dprobs - attn_delta[:, :, None])
    grad_value = jnp.einsum(
        "hnk,nhd->kd", prob_full, cotangent.astype(jnp.float32), precision=HIGHEST
    )
    grad_key = (
        jnp.einsum("hnk,nhd->kd", dscores, queries.astype(jnp.float32), precision=HIGHEST)
        * score_scale
    )
    group_devices = max(1, (Q_HEADS // KV_HEADS) // local_heads)
    raw_inputs = (
        gdn_q.astype(jnp.float32),
        gdn_k.astype(jnp.float32),
        gdn_v.astype(jnp.float32),
        decay_logit,
        write_logit,
    )
    value_heads = gdn_v.shape[1] // GDIM
    zero_memory = jnp.zeros((value_heads, GDIM, GDIM), jnp.float32)
    unit_memory = jnp.broadcast_to(jnp.eye(GDIM, dtype=jnp.float32), zero_memory.shape)

    def local_run(raw_values, memory):
        return delta_forward(raw_values, memory, decay_rate, write_scale)

    silent_inputs = (
        raw_inputs[0],
        raw_inputs[1],
        jnp.zeros_like(raw_inputs[2]),
        raw_inputs[3],
        raw_inputs[4],
    )
    transition = local_run(silent_inputs, unit_memory)[1]
    outputs_zero, pull_zero = jax.vjp(local_run, raw_inputs, zero_memory)
    written_end = outputs_zero[1]
    cot_full = gdn_cot.astype(jnp.float32)
    local_grad = pull_zero((cot_full, zero_memory))[1]
    memory_in, memory_grad, (grad_q, group_sums) = exclusive_scans(
        (transition, written_end),
        (jnp.swapaxes(transition, 1, 2), local_grad),
        "ctx",
        compose_maps,
        (grad_q, (grad_key, grad_value)),
    )
    group_sums = butterfly_sum(group_sums, "head", 1, group_devices)
    slot_mask = (jnp.arange(KV_HEADS) == kv_group)[None, :, None]
    key_slots = jnp.where(slot_mask, group_sums[0][:, None, :], 0.0).reshape(tok_rows, KV_HEADS * HD)
    value_slots = jnp.where(slot_mask, group_sums[1][:, None, :], 0.0).reshape(
        tok_rows, KV_HEADS * HD
    )
    attn_dk, attn_dv = butterfly_sum(
        (key_slots, value_slots), "head", group_devices, lax.axis_size("head")
    )
    memory_in, memory_grad, grad_q, attn_dk, attn_dv = lax.optimization_barrier(
        (memory_in, memory_grad, grad_q, attn_dk, attn_dv)
    )
    unused_out, pull_final = jax.vjp(local_run, raw_inputs, memory_in)
    grads = pull_final((cot_full, memory_grad))[0]
    return (grad_q, attn_dk, attn_dv, grads[0], grads[1], grads[2], grads[3], grads[4])


def solution(mesh):
    return jax.shard_map(
        on_device,
        mesh=mesh,
        in_specs=(
            P("ctx", "head"),
            P("ctx", None),
            P("ctx", None),
            P("ctx", "head"),
            P("head", None),
            P("head", None),
            P("head", None, None),
            P("ctx", "head"),
            P("ctx", "head"),
            P("ctx", "head"),
            P("head", "ctx"),
            P("head", "ctx"),
            P("head"),
            P("head"),
            P("ctx", "head"),
        ),
        out_specs=(
            P("ctx", "head"),
            P("ctx", None),
            P("ctx", None),
            P("ctx", "head"),
            P("ctx", "head"),
            P("ctx", "head"),
            P("head", "ctx"),
            P("head", "ctx"),
        ),
        check_vma=False,
    )
```
